128 devices in a mesh: dp: 8 (over z_hi, y), expert: 16 (over x, z_lo, core).
Axes of the slice: x: 4, y: 4, z: 4 (z_hi: 2, z_lo: 2; z = z_hi * 2 + z_lo), core: 2. Of those that a mesh axis runs over, the one named last changes fastest.
Arguments:
- tokens: bfloat16 [16384, 2880], P(('dp', 'expert')), may hold values from -6 to 6
- expert_ids: int32 [16384, 4], P(('dp', 'expert')), may hold values from 0 to 15, all different within a row; in each aligned block of 128 rows (0 to 127, 128 to 255, ...) at most 64 rows name the same one
- gates: bfloat16 [16384, 4], P(('dp', 'expert')), may hold values from 0.099609375 to 1
- w_gate: bfloat16 [16, 2880, 1440], P('expert'), may hold values from -0.109375 to 0.109375
- w_up: bfloat16 [16, 2880, 1440], P('expert'), may hold values from -0.109375 to 0.109375
- w_down: bfloat16 [16, 1440, 2880], P('expert'), may hold values from -0.15625 to 0.15625
Outputs:
- mixed: bfloat16 [16384, 2880], P(('dp', 'expert'))
- expert_load: int32 [16], replicated
The draws below stay inside these ranges and needn't reach their ends.
Inputs may be any that keep to these rules, and one draw needn't show every extreme that they name: `expert_ids`: each token names 4 different experts. Among the rows of one device (aligned blocks of 128 rows) every expert is named by at most 64 rows, a bound that some block reaches.
All inputs are finite; a program needn't handle non-finite values.
Results may differ from the reference program's by a relative error of at most 0.004.
The reference program's roundings to bfloat16 on the way (of `hidden`) count: a program that leaves them out, or rounds other values in their place, can miss the bound.
Values may be sent and summed in bfloat16 or wider, within the bound.
No kernel may reach another device: no remote copies, remote signals or barrier semaphores. Data moves between devices by JAX's collectives and lax.ppermute only.
A program may use at most 192 MiB of HBM per device.

```python
import math
import jax
import jax.numpy as jnp
import numpy as np
from jax import lax

D = 2880
FF = 1440
TOP = 4
BLOCK = 128
TOK_DEV = 128
EXPERTS = 16
TOKENS = 16384
SRC_CAP = 64
CAP = 1024
N_DP = 8


def block_scale(rng, dims, split, least, largest):
    def one(dim, shards_of):
        draws = jax.random.uniform(jax.random.fold_in(jax.random.fold_in(rng, 6), dim), (shards_of,), jnp.float32, least / len(split), largest / len(split))
        return jnp.repeat(jnp.exp(draws), dims[dim] // shards_of).reshape((-1,) + (1,) * (len(dims) - dim - 1))

    factor_of = one(*split[0])
    for cut in split[1:]:
        factor_of = factor_of * one(*cut)
    return factor_of


def shared_out(own_key, own, number, rows, amount, top, bound, lean):
    order = jax.random.permutation(own_key, amount)
    crowded, ordinary = portions_of(amount, rows * top, bound, lean, True), portions_of(amount, rows * top, bound, lean, False)
    places = jnp.arange(amount)

    def named(tallies, offset_by):
        used = int((tallies > 0).sum())
        fixed = max(1, used // 4)
        moved = fixed + (places - fixed + offset_by * (used - fixed)) % max(1, amount - fixed)
        return jnp.zeros((amount,), jnp.int32).at[order[jnp.where(places < fixed, places, moved)]].set(jnp.asarray(tallies, jnp.int32))

    tallies = jnp.where(number % 4 == 0, named(crowded, number // 4), named(ordinary, number - number // 4 - 1))
    mixed = jax.random.permutation(jax.random.fold_in(own, 3), amount)
    donor, sink = mixed[0:amount // 2 * 2:2], mixed[1:amount // 2 * 2:2]
    room = jnp.minimum(tallies[donor] - 1, bound - tallies[sink]) // 2
    room = jnp.where((donor == order[0]) | (sink == order[0]) | (tallies[sink] == 0), 0, jnp.maximum(room, 0))
    moved = jax.random.randint(jax.random.fold_in(own, 4), (amount // 2,), 0, 1 << 20) % (room + 1)
    tallies = tallies.at[donor].add(-moved).at[sink].add(moved)
    members = jnp.searchsorted(jnp.cumsum(tallies), jnp.arange(rows * top), side="right").astype(jnp.int32)
    grid = members.reshape(top, rows).T
    grid = grid[jax.random.permutation(jax.random.fold_in(own, 1), rows)]
    offset_by = jax.random.randint(jax.random.fold_in(own, 2), (rows, 1), 0, top)
    return jnp.take_along_axis(grid, (jnp.arange(top)[None, :] + offset_by) % top, axis=1)


def portions_of(number_of, total, limit, skew, full):
    portions = [(1 << 20) // math.isqrt(grade ** skew) + 1 for grade in range(1, number_of + 1)]
    largest = limit if full else min(limit, max(-(-total // number_of), total * portions[0] // sum(portions)))
    least = 1 if total - largest >= number_of - 1 else 0
    given, rest = [largest] + [least] * (number_of - 1), total - largest - least * (number_of - 1)
    while rest > 0:
        movable = [i for i in range(1, number_of) if given[i] < largest] or [i for i in range(1, number_of) if given[i] < limit]
        pool, budget = sum([portions[i] for i in movable]), rest
        for i in movable:
            addition = min(limit - given[i], max(1, budget * portions[i] // pool), rest)
            given[i] = given[i] + addition
            rest = rest - addition
    return np.array(given)


def noise(rng, dims, deviation, reach, pieces=(), kind=jnp.bfloat16):
    values = jax.random.normal(rng, dims, jnp.float32) * deviation
    if len(pieces) > 0:
        values = block_scale(rng, dims, pieces, -0.22, 0.18) * values
    return jnp.clip(values, min=-reach, max=reach).astype(kind)


def setup_inputs(seed: int = 0) -> dict:
    seeds = jax.random.split(jax.random.key(seed), 7)
    tokens = noise(seeds[0], (TOKENS, D), 1.0, 6.0, ((0, 128),))
    expert_ids_keys = jax.random.split(jax.random.fold_in(seeds[1], 1), TOKENS // TOK_DEV)
    expert_ids_turns = jax.random.permutation(jax.random.fold_in(seeds[1], 3), TOKENS // TOK_DEV)
    expert_ids = jax.vmap(lambda own, number: shared_out(jax.random.fold_in(seeds[1], 2), own, number, TOK_DEV, EXPERTS, TOP, SRC_CAP, 2))(expert_ids_keys, expert_ids_turns).reshape((TOKENS, TOP))
    gates = jnp.clip(0.099609375 + 0.9003906 * jax.random.uniform(seeds[2], (TOKENS, TOP), jnp.float32) ** block_scale(seeds[2], (TOKENS, TOP), ((0, 128),), -0.2, 0.2), 0.099609375, 1.0).astype(jnp.bfloat16)
    w_gate = noise(seeds[3], (EXPERTS, D, FF), D ** -0.5, 0.109375, ((0, 16),))
    w_up = noise(seeds[4], (EXPERTS, D, FF), D ** -0.5, 0.109375, ((0, 16),))
    w_down = noise(seeds[5], (EXPERTS, FF, D), FF ** -0.5, 0.15625, ((0, 16),))
    return dict(tokens=tokens, expert_ids=expert_ids, gates=gates, w_gate=w_gate, w_up=w_up, w_down=w_down)


def reference(tokens, expert_ids, gates, w_gate, w_up, w_down):
    total = tokens.shape[0]
    buffer = N_DP * CAP
    onehot = expert_ids[:, :, None] == jnp.arange(EXPERTS, dtype=jnp.int32)[None, None, :]
    table = jnp.sum(gates.astype(jnp.float32)[:, :, None] * onehot.astype(jnp.float32), axis=1)
    token_index = jnp.arange(total, dtype=jnp.int32)

    def per_expert(expert, mixed_sum):
        column = lax.dynamic_index_in_dim(table, expert, 1, keepdims=False)
        routed = column > 0
        position = jnp.cumsum(routed.astype(jnp.int32)) - 1
        count = jnp.sum(routed.astype(jnp.int32))
        target = jnp.where(routed, position, buffer).astype(jnp.int32)
        slot_tok = jnp.zeros((buffer,), jnp.int32).at[target].set(token_index, mode="drop")
        slot_weight = jnp.where(jnp.arange(buffer, dtype=jnp.int32) < count, column[slot_tok], jnp.float32(0.0))
        gate_mat = lax.dynamic_index_in_dim(w_gate, expert, 0, keepdims=False)
        up_mat = lax.dynamic_index_in_dim(w_up, expert, 0, keepdims=False)
        down_mat = lax.dynamic_index_in_dim(w_down, expert, 0, keepdims=False)
        blocks = (count + BLOCK - 1) // BLOCK

        def per_block(index, acc):
            rows_idx = lax.dynamic_slice_in_dim(slot_tok, (index * BLOCK).astype(jnp.int32), BLOCK)
            weight = lax.dynamic_slice_in_dim(slot_weight, (index * BLOCK).astype(jnp.int32), BLOCK)
            rows = tokens[rows_idx]
            gate_val = jnp.dot(rows, gate_mat, preferred_element_type=jnp.float32)
            up_val = jnp.dot(rows, up_mat, preferred_element_type=jnp.float32)
            hidden = (jax.nn.silu(gate_val) * up_val).astype(jnp.bfloat16)
            result = jnp.dot(hidden, down_mat, preferred_element_type=jnp.float32)
            return acc.at[rows_idx].add(result * weight[:, None])

        return lax.fori_loop(jnp.int32(0), blocks.astype(jnp.int32), per_block, mixed_sum)

    mixed_sum = lax.fori_loop(0, EXPERTS, per_expert, jnp.zeros((total, D), jnp.float32))
    expert_load = jnp.sum(onehot.astype(jnp.int32), axis=(0, 1)).astype(jnp.int32)
    return mixed_sum.astype(jnp.bfloat16), expert_load
```

```python
import jax
import jax.numpy as jnp
from jax import lax
from jax.sharding import PartitionSpec as P

SRC_CAP = 64


def split3(value):
    hi = value.astype(jnp.bfloat16)
    rest = value - hi.astype(jnp.float32)
    mid = rest.astype(jnp.bfloat16)
    lo = (rest - mid.astype(jnp.float32)).astype(jnp.bfloat16)
    return hi, mid, lo


def shards(tokens, expert_ids, gates, w_gate, w_up, w_down):
    tok_rows, width = tokens.shape
    n_experts = lax.axis_size("expert")
    cap = SRC_CAP
    experts = jnp.arange(n_experts, dtype=jnp.int32)
    onehot = expert_ids[:, :, None] == experts[None, None, :]
    routed = jnp.any(onehot, axis=1)
    position = jnp.cumsum(routed.astype(jnp.int32), axis=0) - 1
    slots = jnp.arange(cap, dtype=jnp.int32)
    pick = routed.T[:, None, :] & (position.T[:, None, :] == slots[None, :, None])
    pick = pick.reshape(n_experts * cap, tok_rows)
    send = jnp.dot(pick.astype(jnp.bfloat16), tokens, preferred_element_type=jnp.float32)
    send = send.astype(jnp.bfloat16).reshape(n_experts, cap, width)
    rows = lax.all_to_all(send, "expert", 0, 0, tiled=True).reshape(n_experts * cap, width)

    gate_val = jnp.dot(rows, w_gate[0], preferred_element_type=jnp.float32)
    up_val = jnp.dot(rows, w_up[0], preferred_element_type=jnp.float32)
    hidden = (jax.nn.silu(gate_val) * up_val).astype(jnp.bfloat16)
    result = jnp.dot(hidden, w_down[0], preferred_element_type=jnp.float32)

    back = lax.all_to_all(result.reshape(n_experts, cap, width), "expert", 0, 0, tiled=True)
    back = back.reshape(n_experts * cap, width)
    table = jnp.sum(gates.astype(jnp.float32)[:, :, None] * onehot.astype(jnp.float32), axis=1)
    weight = jnp.where(pick.T.reshape(tok_rows, n_experts, cap), table[:, :, None], 0.0)
    weight = weight.reshape(tok_rows, n_experts * cap).astype(jnp.bfloat16)
    mixed = sum(
        jnp.dot(weight, piece, preferred_element_type=jnp.float32) for piece in split3(back)
    ).astype(jnp.bfloat16)

    local_load = jnp.sum(onehot.astype(jnp.int32), axis=(0, 1))
    expert_load = lax.psum(local_load, ("dp", "expert"))
    return (mixed, expert_load)


def solution(mesh):
    placed = (
        P(("dp", "expert"), None),
        P(("dp", "expert"), None),
        P(("dp", "expert"), None),
        P("expert", None, None),
        P("expert", None, None),
        P("expert", None, None),
    )
    return jax.shard_map(
        shards,
        mesh=mesh,
        in_specs=placed,
        out_specs=(P(("dp", "expert"), None), P()),
        check_vma=False,
    )
```

```python
import jax
import jax.numpy as jnp
from jax import lax
from jax.sharding import PartitionSpec as P

SRC_CAP = 64


def split2(value):
    hi = value.astype(jnp.bfloat16)
    lo = (value - hi.astype(jnp.float32)).astype(jnp.bfloat16)
    return jnp.stack([hi, lo], axis=1)


def shards(tokens, expert_ids, gates, w_gate, w_up, w_down):
    tok_rows, width = tokens.shape
    n_experts = lax.axis_size("expert")
    cap = SRC_CAP
    experts = jnp.arange(n_experts, dtype=jnp.int32)
    onehot = expert_ids[:, :, None] == experts[None, None, :]
    local_load = jnp.sum(onehot.astype(jnp.int32), axis=(0, 1))
    expert_load = lax.psum(local_load, ("dp", "expert"))
    expert_load, tokens = lax.optimization_barrier((expert_load, tokens))
    routed = jnp.any(onehot, axis=1)
    position = jnp.cumsum(routed.astype(jnp.int32), axis=0) - 1
    slots = jnp.arange(cap, dtype=jnp.int32)
    pick = routed.T[:, None, :] & (position.T[:, None, :] == slots[None, :, None])
    pick = pick.reshape(n_experts * cap, tok_rows)
    send = jnp.dot(pick.astype(jnp.bfloat16), tokens, preferred_element_type=jnp.float32)
    send = send.astype(jnp.bfloat16).reshape(n_experts, cap, width)
    rows = lax.all_to_all(send, "expert", 0, 0, tiled=True).reshape(n_experts * cap, width)

    gate_val = jnp.dot(rows, w_gate[0], preferred_element_type=jnp.float32)
    up_val = jnp.dot(rows, w_up[0], preferred_element_type=jnp.float32)
    hidden = (jax.nn.silu(gate_val) * up_val).astype(jnp.bfloat16)
    result = jnp.dot(hidden, w_down[0], preferred_element_type=jnp.float32)

    pieces = split2(result.reshape(n_experts, cap, width))
    back = lax.all_to_all(pieces, "expert", 0, 0, tiled=True)
    table = jnp.sum(gates.astype(jnp.float32)[:, :, None] * onehot.astype(jnp.float32), axis=1)
    weight = jnp.where(pick.T.reshape(tok_rows, n_experts, cap), table[:, :, None], 0.0)
    weight = weight.reshape(tok_rows, n_experts * cap).astype(jnp.bfloat16)
    mixed = (
        jnp.dot(weight, back[:, 0].reshape(n_experts * cap, width), preferred_element_type=jnp.float32)
        + jnp.dot(weight, back[:, 1].reshape(n_experts * cap, width), preferred_element_type=jnp.float32)
    ).astype(jnp.bfloat16)

    return (mixed, expert_load)


def solution(mesh):
    placed = (
        P(("dp", "expert"), None),
        P(("dp", "expert"), None),
        P(("dp", "expert"), None),
        P("expert", None, None),
        P("expert", None, None),
        P("expert", None, None),
    )
    return jax.shard_map(
        shards,
        mesh=mesh,
        in_specs=placed,
        out_specs=(P(("dp", "expert"), None), P()),
        check_vma=False,
    )
```

```python
import jax
import jax.numpy as jnp
from jax import lax
from jax.sharding import PartitionSpec as P

SRC_CAP = 64


def split2(value):
    hi = value.astype(jnp.bfloat16)
    lo = (value - hi.astype(jnp.float32)).astype(jnp.bfloat16)
    return hi, lo


def tree_sum(value):
    n_dev = lax.axis_size("dp") * lax.axis_size("expert")
    step = 1
    while step < n_dev:
        perm = [(i, i ^ step) for i in range(n_dev)]
        value = value + lax.ppermute(value, ("dp", "expert"), perm)
        step *= 2
    return value


def shards(tokens, expert_ids, gates, w_gate, w_up, w_down):
    tok_rows, width = tokens.shape
    n_experts = lax.axis_size("expert")
    cap = SRC_CAP
    experts = jnp.arange(n_experts, dtype=jnp.int32)
    onehot = expert_ids[:, :, None] == experts[None, None, :]
    expert_load = tree_sum(jnp.sum(onehot.astype(jnp.int32), axis=(0, 1)))
    routed = jnp.any(onehot, axis=1)
    position = jnp.cumsum(routed.astype(jnp.int32), axis=0) - 1
    slots = jnp.arange(cap, dtype=jnp.int32)
    pick = routed.T[:, None, :] & (position.T[:, None, :] == slots[None, :, None])
    pick = pick.reshape(n_experts * cap, tok_rows)
    send = jnp.dot(pick.astype(jnp.bfloat16), tokens, preferred_element_type=jnp.float32)
    send = send.astype(jnp.bfloat16).reshape(n_experts, cap, width)
    rows = lax.all_to_all(send, "expert", 0, 0, tiled=True).reshape(n_experts * cap, width)

    gate_val = jnp.dot(rows, w_gate[0], preferred_element_type=jnp.float32)
    up_val = jnp.dot(rows, w_up[0], preferred_element_type=jnp.float32)
    hidden = (jax.nn.silu(gate_val) * up_val).astype(jnp.bfloat16)
    result = jnp.dot(hidden, w_down[0], preferred_element_type=jnp.float32)

    hi, lo = split2(result.reshape(n_experts, cap, width))
    back_hi = lax.all_to_all(hi, "expert", 0, 0, tiled=True).reshape(n_experts * cap, width)
    back_lo = lax.all_to_all(lo, "expert", 0, 0, tiled=True).reshape(n_experts * cap, width)
    table = jnp.sum(gates.astype(jnp.float32)[:, :, None] * onehot.astype(jnp.float32), axis=1)
    weight = jnp.where(pick.T.reshape(tok_rows, n_experts, cap), table[:, :, None], 0.0)
    weight = weight.reshape(tok_rows, n_experts * cap).astype(jnp.bfloat16)
    mixed = (
        jnp.dot(weight, back_hi, preferred_element_type=jnp.float32)
        + jnp.dot(weight, back_lo, preferred_element_type=jnp.float32)
    ).astype(jnp.bfloat16)

    return (mixed, expert_load)


def solution(mesh):
    placed = (
        P(("dp", "expert"), None),
        P(("dp", "expert"), None),
        P(("dp", "expert"), None),
        P("expert", None, None),
        P("expert", None, None),
        P("expert", None, None),
    )
    return jax.shard_map(
        shards,
        mesh=mesh,
        in_specs=placed,
        out_specs=(P(("dp", "expert"), None), P()),
        check_vma=False,
    )
```

```python
import jax
import jax.numpy as jnp
from jax import lax
from jax.sharding import PartitionSpec as P

SRC_CAP = 64
CHUNKS = 2


def split2(value):
    hi = value.astype(jnp.bfloat16)
    lo = (value - hi.astype(jnp.float32)).astype(jnp.bfloat16)
    return hi, lo


def tree_sum(value):
    n_dev = lax.axis_size("dp") * lax.axis_size("expert")
    step = 1
    while step < n_dev:
        perm = [(i, i ^ step) for i in range(n_dev)]
        value = value + lax.ppermute(value, ("dp", "expert"), perm)
        step *= 2
    return value


def shards(tokens, expert_ids, gates, w_gate, w_up, w_down):
    tok_rows, width = tokens.shape
    n_experts = lax.axis_size("expert")
    cap = SRC_CAP
    experts = jnp.arange(n_experts, dtype=jnp.int32)
    onehot = expert_ids[:, :, None] == experts[None, None, :]
    expert_load = tree_sum(jnp.sum(onehot.astype(jnp.int32), axis=(0, 1)))
    expert_load, tokens = lax.optimization_barrier((expert_load, tokens))
    routed = jnp.any(onehot, axis=1)
    position = jnp.cumsum(routed.astype(jnp.int32), axis=0) - 1
    slots = jnp.arange(cap, dtype=jnp.int32)
    pick = routed.T[:, None, :] & (position.T[:, None, :] == slots[None, :, None])
    pick = pick.reshape(n_experts * cap, tok_rows)
    send = jnp.dot(pick.astype(jnp.bfloat16), tokens, preferred_element_type=jnp.float32)
    send = send.astype(jnp.bfloat16).reshape(n_experts, cap, width)
    table = jnp.sum(gates.astype(jnp.float32)[:, :, None] * onehot.astype(jnp.float32), axis=1)
    weight = jnp.where(pick.T.reshape(tok_rows, n_experts, cap), table[:, :, None], 0.0)
    weight = weight.astype(jnp.bfloat16)
    chunk = cap // CHUNKS
    mixed = jnp.zeros((tok_rows, width), jnp.float32)
    for c in range(CHUNKS):
        part = send[:, c * chunk:(c + 1) * chunk]
        rows = lax.all_to_all(part, "expert", 0, 0, tiled=True).reshape(n_experts * chunk, width)
        gate_val = jnp.dot(rows, w_gate[0], preferred_element_type=jnp.float32)
        up_val = jnp.dot(rows, w_up[0], preferred_element_type=jnp.float32)
        hidden = (jax.nn.silu(gate_val) * up_val).astype(jnp.bfloat16)
        result = jnp.dot(hidden, w_down[0], preferred_element_type=jnp.float32)
        hi, lo = split2(result.reshape(n_experts, chunk, width))
        back_hi = lax.all_to_all(hi, "expert", 0, 0, tiled=True).reshape(n_experts * chunk, width)
        back_lo = lax.all_to_all(lo, "expert", 0, 0, tiled=True).reshape(n_experts * chunk, width)
        part_weight = weight[:, :, c * chunk:(c + 1) * chunk].reshape(tok_rows, n_experts * chunk)
        mixed = mixed + jnp.dot(part_weight, back_hi, preferred_element_type=jnp.float32)
        mixed = mixed + jnp.dot(part_weight, back_lo, preferred_element_type=jnp.float32)
    mixed = mixed.astype(jnp.bfloat16)
    return (mixed, expert_load)


def solution(mesh):
    placed = (
        P(("dp", "expert"), None),
        P(("dp", "expert"), None),
        P(("dp", "expert"), None),
        P("expert", None, None),
        P("expert", None, None),
        P("expert", None, None),
    )
    return jax.shard_map(
        shards,
        mesh=mesh,
        in_specs=placed,
        out_specs=(P(("dp", "expert"), None), P()),
        check_vma=False,
    )
```

```python
import jax
import jax.numpy as jnp
from jax import lax
from jax.sharding import PartitionSpec as P

SRC_CAP = 64
CHUNKS = 2


def split2(value):
    hi = value.astype(jnp.bfloat16)
    lo = (value - hi.astype(jnp.float32)).astype(jnp.bfloat16)
    return hi, lo


def tree_sum(value, axis):
    n_dev = lax.axis_size(axis)
    step = 1
    while step < n_dev:
        perm = [(i, i ^ step) for i in range(n_dev)]
        value = value + lax.ppermute(value, axis, perm)
        step *= 2
    return value


def shards(tokens, expert_ids, gates, w_gate, w_up, w_down):
    tok_rows, width = tokens.shape
    n_experts = lax.axis_size("expert")
    cap = SRC_CAP
    experts = jnp.arange(n_experts, dtype=jnp.int32)
    onehot = expert_ids[:, :, None] == experts[None, None, :]
    local_load = jnp.sum(onehot.astype(jnp.int32), axis=(0, 1))
    routed = jnp.any(onehot, axis=1)
    position = jnp.cumsum(routed.astype(jnp.int32), axis=0) - 1
    slots = jnp.arange(cap, dtype=jnp.int32)
    pick = routed.T[:, None, :] & (position.T[:, None, :] == slots[None, :, None])
    pick = pick.reshape(n_experts * cap, tok_rows)
    send = jnp.dot(pick.astype(jnp.bfloat16), tokens, preferred_element_type=jnp.float32)
    send = send.astype(jnp.bfloat16).reshape(n_experts, cap, width)
    table = jnp.sum(gates.astype(jnp.float32)[:, :, None] * onehot.astype(jnp.float32), axis=1)
    weight = jnp.where(pick.T.reshape(tok_rows, n_experts, cap), table[:, :, None], 0.0)
    weight = weight.astype(jnp.bfloat16)
    chunk = cap // CHUNKS
    mixed = jnp.zeros((tok_rows, width), jnp.float32)
    load_row = jnp.zeros((width,), jnp.float32).at[:n_experts].set(local_load.astype(jnp.float32))
    load_rows = jnp.broadcast_to(load_row.astype(jnp.bfloat16), (n_experts, 1, width))
    for c in range(CHUNKS):
        part = send[:, c * chunk:(c + 1) * chunk]
        if c == 0:
            part = jnp.concatenate([part, load_rows], axis=1)
        rows = lax.all_to_all(part, "expert", 0, 0, tiled=True)
        if c == 0:
            group_load = jnp.sum(rows[:, chunk, :n_experts].astype(jnp.float32), axis=0)
            expert_load = tree_sum(group_load.astype(jnp.int32), "dp")
            rows = rows[:, :chunk]
        rows = rows.reshape(n_experts * chunk, width)
        gate_val = jnp.dot(rows, w_gate[0], preferred_element_type=jnp.float32)
        up_val = jnp.dot(rows, w_up[0], preferred_element_type=jnp.float32)
        hidden = (jax.nn.silu(gate_val) * up_val).astype(jnp.bfloat16)
        result = jnp.dot(hidden, w_down[0], preferred_element_type=jnp.float32)
        hi, lo = split2(result.reshape(n_experts, chunk, width))
        back = lax.all_to_all(jnp.concatenate([hi, lo], axis=1), "expert", 0, 0, tiled=True)
        back_hi = back[:, :chunk].reshape(n_experts * chunk, width)
        back_lo = back[:, chunk:].reshape(n_experts * chunk, width)
        part_weight = weight[:, :, c * chunk:(c + 1) * chunk].reshape(tok_rows, n_experts * chunk)
        mixed = mixed + jnp.dot(part_weight, back_hi, preferred_element_type=jnp.float32)
        mixed = mixed + jnp.dot(part_weight, back_lo, preferred_element_type=jnp.float32)
    mixed = mixed.astype(jnp.bfloat16)
    return (mixed, expert_load)


def solution(mesh):
    placed = (
        P(("dp", "expert"), None),
        P(("dp", "expert"), None),
        P(("dp", "expert"), None),
        P("expert", None, None),
        P("expert", None, None),
        P("expert", None, None),
    )
    return jax.shard_map(
        shards,
        mesh=mesh,
        in_specs=placed,
        out_specs=(P(("dp", "expert"), None), P()),
        check_vma=False,
    )
```

```python
import jax
import jax.numpy as jnp
from jax import lax
from jax.sharding import PartitionSpec as P

SRC_CAP = 64
CHUNKS = 2


def split2(value):
    hi = value.astype(jnp.bfloat16)
    lo = (value - hi.astype(jnp.float32)).astype(jnp.bfloat16)
    return hi, lo


def tree_sum(value, axis):
    n_dev = lax.axis_size(axis)
    step = 1
    while step < n_dev:
        perm = [(i, i ^ step) for i in range(n_dev)]
        value = value + lax.ppermute(value, axis, perm)
        step *= 2
    return value


def shards(tokens, expert_ids, gates, w_gate, w_up, w_down):
    tok_rows, width = tokens.shape
    n_experts = lax.axis_size("expert")
    cap = SRC_CAP
    experts = jnp.arange(n_experts, dtype=jnp.int32)
    onehot = expert_ids[:, :, None] == experts[None, None, :]
    local_load = jnp.sum(onehot.astype(jnp.int32), axis=(0, 1))
    routed = jnp.any(onehot, axis=1)
    position = jnp.cumsum(routed.astype(jnp.int32), axis=0) - 1
    slots = jnp.arange(cap, dtype=jnp.int32)
    pick = routed.T[:, None, :] & (position.T[:, None, :] == slots[None, :, None])
    pick = pick.reshape(n_experts * cap, tok_rows)
    send = jnp.dot(pick.astype(jnp.bfloat16), tokens, preferred_element_type=jnp.float32)
    send = send.astype(jnp.bfloat16).reshape(n_experts, cap, width)
    table = jnp.sum(gates.astype(jnp.float32)[:, :, None] * onehot.astype(jnp.float32), axis=1)
    weight = jnp.where(pick.T.reshape(tok_rows, n_experts, cap), table[:, :, None], 0.0)
    weight = weight.astype(jnp.bfloat16)
    chunk = cap // CHUNKS
    mixed = jnp.zeros((tok_rows, width), jnp.float32)
    load_row = jnp.zeros((width,), jnp.float32).at[:n_experts].set(local_load.astype(jnp.float32))
    load_rows = jnp.broadcast_to(load_row.astype(jnp.bfloat16), (n_experts, 1, width))
    for c in range(CHUNKS):
        part = send[:, c * chunk:(c + 1) * chunk]
        if c == 0:
            part = jnp.concatenate([part, load_rows], axis=1)
        rows = lax.all_to_all(part, "expert", 0, 0, tiled=True)
        if c == 0:
            group_load = jnp.sum(rows[:, chunk, :n_experts].astype(jnp.float32), axis=0)
            expert_load = tree_sum(group_load.astype(jnp.int32), "dp")
            rows = rows[:, :chunk]
        rows = rows.reshape(n_experts * chunk, width)
        gate_val = jnp.dot(rows, w_gate[0], preferred_element_type=jnp.float32)
        up_val = jnp.dot(rows, w_up[0], preferred_element_type=jnp.float32)
        hidden = (jax.nn.silu(gate_val) * up_val).astype(jnp.bfloat16)
        result = jnp.dot(hidden, w_down[0], preferred_element_type=jnp.float32)
        hi, lo = split2(result.reshape(n_experts, chunk, width))
        back_hi = lax.all_to_all(hi, "expert", 0, 0, tiled=True).reshape(n_experts * chunk, width)
        back_lo = lax.all_to_all(lo, "expert", 0, 0, tiled=True).reshape(n_experts * chunk, width)
        part_weight = weight[:, :, c * chunk:(c + 1) * chunk].reshape(tok_rows, n_experts * chunk)
        mixed = mixed + jnp.dot(part_weight, back_hi, preferred_element_type=jnp.float32)
        mixed = mixed + jnp.dot(part_weight, back_lo, preferred_element_type=jnp.float32)
    mixed = mixed.astype(jnp.bfloat16)
    return (mixed, expert_load)


def solution(mesh):
    placed = (
        P(("dp", "expert"), None),
        P(("dp", "expert"), None),
        P(("dp", "expert"), None),
        P("expert", None, None),
        P("expert", None, None),
        P("expert", None, None),
    )
    return jax.shard_map(
        shards,
        mesh=mesh,
        in_specs=placed,
        out_specs=(P(("dp", "expert"), None), P()),
        check_vma=False,
    )
```

```python
import jax
import jax.numpy as jnp
from jax import lax
from jax.experimental import pallas as pl
from jax.sharding import PartitionSpec as P

SRC_CAP = 64
CHUNKS = 2


def split2(value):
    hi = value.astype(jnp.bfloat16)
    lo = (value - hi.astype(jnp.float32)).astype(jnp.bfloat16)
    return hi, lo


def tree_sum(value, axis):
    n_dev = lax.axis_size(axis)
    step = 1
    while step < n_dev:
        perm = [(i, i ^ step) for i in range(n_dev)]
        value = value + lax.ppermute(value, axis, perm)
        step *= 2
    return value


def pack_kernel(pick_ref, tok_ref, load_ref, first_ref, second_ref):
    n_experts, cap, _ = pick_ref.shape
    chunk = cap // 2
    tok = tok_ref[...]
    load = load_ref[...]
    for e in range(n_experts):
        packed = jnp.dot(pick_ref[e], tok, preferred_element_type=jnp.float32).astype(tok.dtype)
        first_ref[e, :chunk, :] = packed[:chunk]
        first_ref[e, chunk:, :] = load
        second_ref[e] = packed[chunk:]


def pack(pick, tokens, load_row):
    n_experts, cap, _ = pick.shape
    width = tokens.shape[1]
    chunk = cap // 2
    return pl.pallas_call(
        pack_kernel,
        out_shape=(
            jax.ShapeDtypeStruct((n_experts, chunk + 1, width), tokens.dtype),
            jax.ShapeDtypeStruct((n_experts, chunk, width), tokens.dtype),
        ),
    )(pick, tokens, load_row)


def shards(tokens, expert_ids, gates, w_gate, w_up, w_down):
    tok_rows, width = tokens.shape
    n_experts = lax.axis_size("expert")
    cap = SRC_CAP
    experts = jnp.arange(n_experts, dtype=jnp.int32)
    onehot = expert_ids[:, :, None] == experts[None, None, :]
    routed = jnp.any(onehot, axis=1)
    position = jnp.cumsum(routed.astype(jnp.int32), axis=0) - 1
    slots = jnp.arange(cap, dtype=jnp.int32)
    pick = routed.T[:, None, :] & (position.T[:, None, :] == slots[None, :, None])
    local_load = jnp.sum(onehot.astype(jnp.int32), axis=(0, 1))
    load_row = jnp.zeros((1, width), jnp.float32).at[0, :n_experts].set(local_load.astype(jnp.float32))
    sends = pack(pick.astype(jnp.bfloat16), tokens, load_row.astype(jnp.bfloat16))
    table = jnp.sum(gates.astype(jnp.float32)[:, :, None] * onehot.astype(jnp.float32), axis=1)
    weight = jnp.where(jnp.transpose(pick, (2, 0, 1)), table[:, :, None], 0.0)
    weight = weight.astype(jnp.bfloat16)
    chunk = cap // CHUNKS
    mixed = jnp.zeros((tok_rows, width), jnp.float32)
    for c in range(CHUNKS):
        rows = lax.all_to_all(sends[c], "expert", 0, 0, tiled=True)
        if c == 0:
            group_load = jnp.sum(rows[:, chunk, :n_experts].astype(jnp.float32), axis=0)
            expert_load = tree_sum(group_load.astype(jnp.int32), "dp")
            rows = rows[:, :chunk]
        rows = rows.reshape(n_experts * chunk, width)
        gate_val = jnp.dot(rows, w_gate[0], preferred_element_type=jnp.float32)
        up_val = jnp.dot(rows, w_up[0], preferred_element_type=jnp.float32)
        hidden = (jax.nn.silu(gate_val) * up_val).astype(jnp.bfloat16)
        result = jnp.dot(hidden, w_down[0], preferred_element_type=jnp.float32)
        hi, lo = split2(result.reshape(n_experts, chunk, width))
        back_hi = lax.all_to_all(hi, "expert", 0, 0, tiled=True).reshape(n_experts * chunk, width)
        back_lo = lax.all_to_all(lo, "expert", 0, 0, tiled=True).reshape(n_experts * chunk, width)
        part_weight = weight[:, :, c * chunk:(c + 1) * chunk].reshape(tok_rows, n_experts * chunk)
        mixed = mixed + jnp.dot(part_weight, back_hi, preferred_element_type=jnp.float32)
        mixed = mixed + jnp.dot(part_weight, back_lo, preferred_element_type=jnp.float32)
    mixed = mixed.astype(jnp.bfloat16)
    return (mixed, expert_load)


def solution(mesh):
    placed = (
        P(("dp", "expert"), None),
        P(("dp", "expert"), None),
        P(("dp", "expert"), None),
        P("expert", None, None),
        P("expert", None, None),
        P("expert", None, None),
    )
    return jax.shard_map(
        shards,
        mesh=mesh,
        in_specs=placed,
        out_specs=(P(("dp", "expert"), None), P()),
        check_vma=False,
    )
```

```python
import jax
import jax.numpy as jnp
from jax import lax
from jax.experimental import pallas as pl
from jax.sharding import PartitionSpec as P

SRC_CAP = 64
CHUNKS = 1


def split2(value):
    hi = value.astype(jnp.bfloat16)
    lo = (value - hi.astype(jnp.float32)).astype(jnp.bfloat16)
    return hi, lo


def tree_sum(value, axis):
    n_dev = lax.axis_size(axis)
    step = 1
    while step < n_dev:
        perm = [(i, i ^ step) for i in range(n_dev)]
        value = value + lax.ppermute(value, axis, perm)
        step *= 2
    return value


def pack_kernel(pick_ref, tok_ref, load_ref, *out_refs):
    n_experts, cap, _ = pick_ref.shape
    chunk = cap // len(out_refs)
    tok = tok_ref[...]
    load = load_ref[...]
    for e in range(n_experts):
        packed = jnp.dot(pick_ref[e], tok, preferred_element_type=jnp.float32).astype(tok.dtype)
        for c, out_ref in enumerate(out_refs):
            out_ref[e, :chunk, :] = packed[c * chunk:(c + 1) * chunk]
        out_refs[0][e, chunk:, :] = load


def pack(pick, tokens, load_row):
    n_experts, cap, _ = pick.shape
    width = tokens.shape[1]
    chunk = cap // CHUNKS
    shapes = [jax.ShapeDtypeStruct((n_experts, chunk + 1, width), tokens.dtype)]
    shapes += [jax.ShapeDtypeStruct((n_experts, chunk, width), tokens.dtype)] * (CHUNKS - 1)
    return pl.pallas_call(pack_kernel, out_shape=tuple(shapes))(pick, tokens, load_row)


def shards(tokens, expert_ids, gates, w_gate, w_up, w_down):
    tok_rows, width = tokens.shape
    n_experts = lax.axis_size("expert")
    cap = SRC_CAP
    experts = jnp.arange(n_experts, dtype=jnp.int32)
    onehot = expert_ids[:, :, None] == experts[None, None, :]
    routed = jnp.any(onehot, axis=1)
    position = jnp.cumsum(routed.astype(jnp.int32), axis=0) - 1
    slots = jnp.arange(cap, dtype=jnp.int32)
    pick = routed.T[:, None, :] & (position.T[:, None, :] == slots[None, :, None])
    local_load = jnp.sum(onehot.astype(jnp.int32), axis=(0, 1))
    load_row = jnp.zeros((1, width), jnp.float32).at[0, :n_experts].set(local_load.astype(jnp.float32))
    sends = pack(pick.astype(jnp.bfloat16), tokens, load_row.astype(jnp.bfloat16))
    table = jnp.sum(gates.astype(jnp.float32)[:, :, None] * onehot.astype(jnp.float32), axis=1)
    weight = jnp.where(jnp.transpose(pick, (2, 0, 1)), table[:, :, None], 0.0)
    weight = weight.astype(jnp.bfloat16)
    chunk = cap // CHUNKS
    mixed = jnp.zeros((tok_rows, width), jnp.float32)
    for c in range(CHUNKS):
        rows = lax.all_to_all(sends[c], "expert", 0, 0, tiled=True)
        if c == 0:
            group_load = jnp.sum(rows[:, chunk, :n_experts].astype(jnp.float32), axis=0)
            expert_load = tree_sum(group_load.astype(jnp.int32), "dp")
            rows = rows[:, :chunk]
        rows = rows.reshape(n_experts * chunk, width)
        gate_val = jnp.dot(rows, w_gate[0], preferred_element_type=jnp.float32)
        up_val = jnp.dot(rows, w_up[0], preferred_element_type=jnp.float32)
        hidden = (jax.nn.silu(gate_val) * up_val).astype(jnp.bfloat16)
        result = jnp.dot(hidden, w_down[0], preferred_element_type=jnp.float32)
        hi, lo = split2(result.reshape(n_experts, chunk, width))
        back_hi = lax.all_to_all(hi, "expert", 0, 0, tiled=True).reshape(n_experts * chunk, width)
        back_lo = lax.all_to_all(lo, "expert", 0, 0, tiled=True).reshape(n_experts * chunk, width)
        part_weight = weight[:, :, c * chunk:(c + 1) * chunk].reshape(tok_rows, n_experts * chunk)
        mixed = mixed + jnp.dot(part_weight, back_hi, preferred_element_type=jnp.float32)
        mixed = mixed + jnp.dot(part_weight, back_lo, preferred_element_type=jnp.float32)
    mixed = mixed.astype(jnp.bfloat16)
    return (mixed, expert_load)


def solution(mesh):
    placed = (
        P(("dp", "expert"), None),
        P(("dp", "expert"), None),
        P(("dp", "expert"), None),
        P("expert", None, None),
        P("expert", None, None),
        P("expert", None, None),
    )
    return jax.shard_map(
        shards,
        mesh=mesh,
        in_specs=placed,
        out_specs=(P(("dp", "expert"), None), P()),
        check_vma=False,
    )
```

```python
import jax
import jax.numpy as jnp
from jax import lax
from jax.experimental import pallas as pl
from jax.sharding import PartitionSpec as P

SRC_CAP = 64
CHUNKS = 2


def split2(value):
    hi = value.astype(jnp.bfloat16)
    lo = (value - hi.astype(jnp.float32)).astype(jnp.bfloat16)
    return hi, lo


def tree_sum(value, axis):
    n_dev = lax.axis_size(axis)
    step = 1
    while step < n_dev:
        perm = [(i, i ^ step) for i in range(n_dev)]
        value = value + lax.ppermute(value, axis, perm)
        step *= 2
    return value


def pack_kernel(pick_ref, tok_ref, load_ref, first_ref, second_ref):
    n_experts, cap, _ = pick_ref.shape
    chunk = cap // 2
    width = second_ref.shape[2]
    tok = tok_ref[...]
    load = load_ref[...]
    for e in range(n_experts):
        packed = jnp.dot(pick_ref[e], tok, preferred_element_type=jnp.float32)
        first_ref[e] = (packed[:chunk] + load).astype(first_ref.dtype)
        second_ref[e] = packed[chunk:, :width].astype(second_ref.dtype)


def pack(pick, tokens, load_row):
    n_experts, cap, _ = pick.shape
    width = tokens.shape[1]
    wide = load_row.shape[1]
    chunk = cap // 2
    return pl.pallas_call(
        pack_kernel,
        out_shape=(
            jax.ShapeDtypeStruct((n_experts, chunk, wide), tokens.dtype),
            jax.ShapeDtypeStruct((n_experts, chunk, width), tokens.dtype),
        ),
    )(pick, jnp.pad(tokens, ((0, 0), (0, wide - width))), load_row)


def shards(tokens, expert_ids, gates, w_gate, w_up, w_down):
    tok_rows, width = tokens.shape
    n_experts = lax.axis_size("expert")
    cap = SRC_CAP
    experts = jnp.arange(n_experts, dtype=jnp.int32)
    onehot = expert_ids[:, :, None] == experts[None, None, :]
    routed = jnp.any(onehot, axis=1)
    position = jnp.cumsum(routed.astype(jnp.int32), axis=0) - 1
    slots = jnp.arange(cap, dtype=jnp.int32)
    pick = routed.T[:, None, :] & (position.T[:, None, :] == slots[None, :, None])
    local_load = jnp.sum(onehot.astype(jnp.int32), axis=(0, 1))
    wide = -(-(width + n_experts) // 128) * 128
    load_row = jnp.zeros((1, wide), jnp.float32).at[0, width:width + n_experts].set(local_load.astype(jnp.float32))
    sends = pack(pick.astype(jnp.bfloat16), tokens, load_row)
    table = jnp.sum(gates.astype(jnp.float32)[:, :, None] * onehot.astype(jnp.float32), axis=1)
    weight = jnp.where(jnp.transpose(pick, (2, 0, 1)), table[:, :, None], 0.0)
    weight = weight.astype(jnp.bfloat16)
    chunk = cap // CHUNKS
    mixed = jnp.zeros((tok_rows, width), jnp.float32)
    for c in range(CHUNKS):
        rows = lax.all_to_all(sends[c], "expert", 0, 0, tiled=True)
        if c == 0:
            group_load = jnp.sum(rows[:, 0, width:width + n_experts].astype(jnp.float32), axis=0)
            expert_load = tree_sum(group_load.astype(jnp.int32), "dp")
            rows = rows[:, :, :width]
        rows = rows.reshape(n_experts * chunk, width)
        gate_val = jnp.dot(rows, w_gate[0], preferred_element_type=jnp.float32)
        up_val = jnp.dot(rows, w_up[0], preferred_element_type=jnp.float32)
        hidden = (jax.nn.silu(gate_val) * up_val).astype(jnp.bfloat16)
        result = jnp.dot(hidden, w_down[0], preferred_element_type=jnp.float32)
        hi, lo = split2(result.reshape(n_experts, chunk, width))
        back_hi = lax.all_to_all(hi, "expert", 0, 0, tiled=True).reshape(n_experts * chunk, width)
        back_lo = lax.all_to_all(lo, "expert", 0, 0, tiled=True).reshape(n_experts * chunk, width)
        part_weight = weight[:, :, c * chunk:(c + 1) * chunk].reshape(tok_rows, n_experts * chunk)
        mixed = mixed + jnp.dot(part_weight, back_hi, preferred_element_type=jnp.float32)
        mixed = mixed + jnp.dot(part_weight, back_lo, preferred_element_type=jnp.float32)
    mixed = mixed.astype(jnp.bfloat16)
    return (mixed, expert_load)


def solution(mesh):
    placed = (
        P(("dp", "expert"), None),
        P(("dp", "expert"), None),
        P(("dp", "expert"), None),
        P("expert", None, None),
        P("expert", None, None),
        P("expert", None, None),
    )
    return jax.shard_map(
        shards,
        mesh=mesh,
        in_specs=placed,
        out_specs=(P(("dp", "expert"), None), P()),
        check_vma=False,
    )
```

```python
import jax
import jax.numpy as jnp
from jax import lax
from jax.experimental import pallas as pl
from jax.sharding import PartitionSpec as P

SRC_CAP = 64
CHUNKS = 2


def split2(value):
    hi = value.astype(jnp.bfloat16)
    lo = (value - hi.astype(jnp.float32)).astype(jnp.bfloat16)
    return hi, lo


def tree_sum(value, axis):
    n_dev = lax.axis_size(axis)
    step = 1
    while step < n_dev:
        perm = [(i, i ^ step) for i in range(n_dev)]
        value = value + lax.ppermute(value, axis, perm)
        step *= 2
    return value


def pack_kernel(pick_ref, tok_ref, load_ref, first_ref, second_ref):
    n_experts, cap, _ = pick_ref.shape
    chunk = cap // 2
    width = second_ref.shape[2]
    tok = tok_ref[...]
    load = load_ref[...]
    for e in range(n_experts):
        packed = jnp.dot(pick_ref[e], tok, preferred_element_type=jnp.float32)
        first_ref[e] = (packed[:chunk] + load).astype(first_ref.dtype)
        second_ref[e] = packed[chunk:, :width].astype(second_ref.dtype)


def pack(pick, tokens, load_row):
    n_experts, cap, _ = pick.shape
    width = tokens.shape[1]
    wide = load_row.shape[1]
    chunk = cap // 2
    return pl.pallas_call(
        pack_kernel,
        out_shape=(
            jax.ShapeDtypeStruct((n_experts, chunk, wide), tokens.dtype),
            jax.ShapeDtypeStruct((n_experts, chunk, width), tokens.dtype),
        ),
    )(pick, jnp.pad(tokens, ((0, 0), (0, wide - width))), load_row)


def shards(tokens, expert_ids, gates, w_gate, w_up, w_down):
    tok_rows, width = tokens.shape
    n_experts = lax.axis_size("expert")
    cap = SRC_CAP
    experts = jnp.arange(n_experts, dtype=jnp.int32)
    onehot = expert_ids[:, :, None] == experts[None, None, :]
    routed = jnp.any(onehot, axis=1)
    position = jnp.cumsum(routed.astype(jnp.int32), axis=0) - 1
    slots = jnp.arange(cap, dtype=jnp.int32)
    pick = routed.T[:, None, :] & (position.T[:, None, :] == slots[None, :, None])
    local_load = jnp.sum(onehot.astype(jnp.int32), axis=(0, 1))
    wide = -(-(width + n_experts) // 128) * 128
    load_row = jnp.zeros((1, wide), jnp.float32).at[0, width:width + n_experts].set(local_load.astype(jnp.float32))
    sends = pack(pick.astype(jnp.bfloat16), tokens, load_row)
    table = jnp.sum(gates.astype(jnp.float32)[:, :, None] * onehot.astype(jnp.float32), axis=1)
    weight = jnp.where(jnp.transpose(pick, (2, 0, 1)), table[:, :, None], 0.0)
    weight = weight.astype(jnp.bfloat16)
    chunk = cap // CHUNKS
    mixed = jnp.zeros((tok_rows, width), jnp.float32)
    def ffn(rows):
        rows = rows.reshape(n_experts * chunk, width)
        gate_val = jnp.dot(rows, w_gate[0], preferred_element_type=jnp.float32)
        up_val = jnp.dot(rows, w_up[0], preferred_element_type=jnp.float32)
        hidden = (jax.nn.silu(gate_val) * up_val).astype(jnp.bfloat16)
        result = jnp.dot(hidden, w_down[0], preferred_element_type=jnp.float32)
        return split2(result.reshape(n_experts, chunk, width))

    def combine(part, c, back):
        part_weight = weight[:, :, c * chunk:(c + 1) * chunk].reshape(tok_rows, n_experts * chunk)
        back = back.reshape(n_experts * chunk, width)
        return part + jnp.dot(part_weight, back, preferred_element_type=jnp.float32)

    first = lax.all_to_all(sends[0], "expert", 0, 0, tiled=True)
    group_load = jnp.sum(first[:, 0, width:width + n_experts].astype(jnp.float32), axis=0)
    expert_load = tree_sum(group_load.astype(jnp.int32), "dp")
    second = lax.all_to_all(sends[1], "expert", 0, 0, tiled=True)
    hi0, lo0 = ffn(first[:, :, :width])
    back_hi0 = lax.all_to_all(hi0, "expert", 0, 0, tiled=True)
    hi1, lo1 = ffn(second)
    both = lax.all_to_all(jnp.concatenate([lo0, hi1], axis=1), "expert", 0, 0, tiled=True)
    mixed = combine(mixed, 0, back_hi0)
    mixed = combine(mixed, 0, both[:, :chunk])
    mixed = combine(mixed, 1, both[:, chunk:])
    mixed = combine(mixed, 1, lax.all_to_all(lo1, "expert", 0, 0, tiled=True))
    mixed = mixed.astype(jnp.bfloat16)
    return (mixed, expert_load)


def solution(mesh):
    placed = (
        P(("dp", "expert"), None),
        P(("dp", "expert"), None),
        P(("dp", "expert"), None),
        P("expert", None, None),
        P("expert", None, None),
        P("expert", None, None),
    )
    return jax.shard_map(
        shards,
        mesh=mesh,
        in_specs=placed,
        out_specs=(P(("dp", "expert"), None), P()),
        check_vma=False,
    )
```

```python
import jax
import jax.numpy as jnp
from jax import lax
from jax.experimental import pallas as pl
from jax.sharding import PartitionSpec as P

SRC_CAP = 64
CHUNKS = 2


def split2(value):
    hi = value.astype(jnp.bfloat16)
    lo = (value - hi.astype(jnp.float32)).astype(jnp.bfloat16)
    return hi, lo


def tree_sum(value, axis):
    n_dev = lax.axis_size(axis)
    step = 1
    while step < n_dev:
        perm = [(i, i ^ step) for i in range(n_dev)]
        value = value + lax.ppermute(value, axis, perm)
        step *= 2
    return value


def pack_kernel(pick_ref, tok_ref, load_ref, first_ref, second_ref):
    chunk = first_ref.shape[1]
    width = second_ref.shape[2]
    packed = lax.dot_general(
        pick_ref[0], tok_ref[...], (((1,), (1,)), ((), ())), preferred_element_type=jnp.float32
    )
    first_ref[0] = (packed[:chunk] + load_ref[...]).astype(first_ref.dtype)
    second_ref[0] = packed[chunk:, :width].astype(second_ref.dtype)


def pack(pick, tokens, load_row):
    n_experts, cap, tok_rows = pick.shape
    width = tokens.shape[1]
    wide = load_row.shape[1]
    chunk = cap // 2
    return pl.pallas_call(
        pack_kernel,
        grid=(n_experts,),
        in_specs=[
            pl.BlockSpec((1, cap, tok_rows), lambda e: (e, 0, 0)),
            pl.BlockSpec((wide, tok_rows), lambda e: (0, 0)),
            pl.BlockSpec((1, wide), lambda e: (0, 0)),
        ],
        out_specs=[
            pl.BlockSpec((1, chunk, wide), lambda e: (e, 0, 0)),
            pl.BlockSpec((1, chunk, width), lambda e: (e, 0, 0)),
        ],
        out_shape=(
            jax.ShapeDtypeStruct((n_experts, chunk, wide), tokens.dtype),
            jax.ShapeDtypeStruct((n_experts, chunk, width), tokens.dtype),
        ),
    )(pick, jnp.pad(tokens.T, ((0, wide - width), (0, 0))), load_row)


def shards(tokens, expert_ids, gates, w_gate, w_up, w_down):
    tok_rows, width = tokens.shape
    n_experts = lax.axis_size("expert")
    cap = SRC_CAP
    experts = jnp.arange(n_experts, dtype=jnp.int32)
    onehot = expert_ids[:, :, None] == experts[None, None, :]
    routed = jnp.any(onehot, axis=1)
    position = jnp.cumsum(routed.astype(jnp.int32), axis=0) - 1
    slots = jnp.arange(cap, dtype=jnp.int32)
    pick = routed.T[:, None, :] & (position.T[:, None, :] == slots[None, :, None])
    local_load = jnp.sum(onehot.astype(jnp.int32), axis=(0, 1))
    wide = -(-(width + n_experts) // 128) * 128
    load_row = jnp.zeros((1, wide), jnp.float32).at[0, width:width + n_experts].set(local_load.astype(jnp.float32))
    sends = pack(pick.astype(jnp.bfloat16), tokens, load_row)
    table = jnp.sum(gates.astype(jnp.float32)[:, :, None] * onehot.astype(jnp.float32), axis=1)
    weight = jnp.where(jnp.transpose(pick, (2, 0, 1)), table[:, :, None], 0.0)
    weight = weight.astype(jnp.bfloat16)
    chunk = cap // CHUNKS
    mixed = jnp.zeros((tok_rows, width), jnp.float32)
    def ffn(rows):
        rows = rows.reshape(n_experts * chunk, width)
        gate_val = jnp.dot(rows, w_gate[0], preferred_element_type=jnp.float32)
        up_val = jnp.dot(rows, w_up[0], preferred_element_type=jnp.float32)
        hidden = (jax.nn.silu(gate_val) * up_val).astype(jnp.bfloat16)
        result = jnp.dot(hidden, w_down[0], preferred_element_type=jnp.float32)
        return split2(result.reshape(n_experts, chunk, width))

    def combine(part, c, back):
        part_weight = weight[:, :, c * chunk:(c + 1) * chunk].reshape(tok_rows, n_experts * chunk)
        back = back.reshape(n_experts * chunk, width)
        return part + jnp.dot(part_weight, back, preferred_element_type=jnp.float32)

    first = lax.all_to_all(sends[0], "expert", 0, 0, tiled=True)
    group_load = jnp.sum(first[:, 0, width:width + n_experts].astype(jnp.float32), axis=0)
    expert_load = tree_sum(group_load.astype(jnp.int32), "dp")
    second = lax.all_to_all(sends[1], "expert", 0, 0, tiled=True)
    hi0, lo0 = ffn(first[:, :, :width])
    back_hi0 = lax.all_to_all(hi0, "expert", 0, 0, tiled=True)
    hi1, lo1 = ffn(second)
    both = lax.all_to_all(jnp.concatenate([lo0, hi1], axis=1), "expert", 0, 0, tiled=True)
    mixed = combine(mixed, 0, back_hi0)
    mixed = combine(mixed, 0, both[:, :chunk])
    mixed = combine(mixed, 1, both[:, chunk:])
    mixed = combine(mixed, 1, lax.all_to_all(lo1, "expert", 0, 0, tiled=True))
    mixed = mixed.astype(jnp.bfloat16)
    return (mixed, expert_load)


def solution(mesh):
    placed = (
        P(("dp", "expert"), None),
        P(("dp", "expert"), None),
        P(("dp", "expert"), None),
        P("expert", None, None),
        P("expert", None, None),
        P("expert", None, None),
    )
    return jax.shard_map(
        shards,
        mesh=mesh,
        in_specs=placed,
        out_specs=(P(("dp", "expert"), None), P()),
        check_vma=False,
    )
```

```python
import jax
import jax.numpy as jnp
from jax import lax
from jax.experimental import pallas as pl
from jax.sharding import PartitionSpec as P

SRC_CAP = 64
CHUNKS = 2


def split2(value):
    hi = value.astype(jnp.bfloat16)
    lo = (value - hi.astype(jnp.float32)).astype(jnp.bfloat16)
    return hi, lo


def tree_sum(value, axis):
    n_dev = lax.axis_size(axis)
    step = 1
    while step < n_dev:
        perm = [(i, i ^ step) for i in range(n_dev)]
        value = value + lax.ppermute(value, axis, perm)
        step *= 2
    return value


def pack_kernel(pick_ref, tok_ref, load_ref, first_ref, second_ref):
    n_experts, cap, _ = pick_ref.shape
    chunk = cap // 2
    width = second_ref.shape[2]
    tok = tok_ref[...]
    load = load_ref[...]
    for e in range(n_experts):
        packed = jnp.dot(pick_ref[e], tok, preferred_element_type=jnp.float32)
        first_ref[e] = (packed[:chunk] + load).astype(first_ref.dtype)
        second_ref[e] = packed[chunk:, :width].astype(second_ref.dtype)


def pack(pick, tokens, load_row):
    n_experts, cap, _ = pick.shape
    width = tokens.shape[1]
    wide = load_row.shape[1]
    chunk = cap // 2
    return pl.pallas_call(
        pack_kernel,
        out_shape=(
            jax.ShapeDtypeStruct((n_experts, chunk, wide), tokens.dtype),
            jax.ShapeDtypeStruct((n_experts, chunk, width), tokens.dtype),
        ),
    )(pick, jnp.pad(tokens, ((0, 0), (0, wide - width))), load_row)


def shards(tokens, expert_ids, gates, w_gate, w_up, w_down):
    tok_rows, width = tokens.shape
    n_experts = lax.axis_size("expert")
    cap = SRC_CAP
    experts = jnp.arange(n_experts, dtype=jnp.int32)
    onehot = expert_ids[:, :, None] == experts[None, None, :]
    routed = jnp.any(onehot, axis=1)
    position = jnp.cumsum(routed.astype(jnp.int32), axis=0) - 1
    slots = jnp.arange(cap, dtype=jnp.int32)
    pick = routed.T[:, None, :] & (position.T[:, None, :] == slots[None, :, None])
    local_load = jnp.sum(onehot.astype(jnp.int32), axis=(0, 1))
    wide = -(-(width + n_experts) // 128) * 128
    load_row = jnp.zeros((1, wide), jnp.float32).at[0, width:width + n_experts].set(local_load.astype(jnp.float32))
    sends = pack(pick.astype(jnp.bfloat16), tokens, load_row)
    table = jnp.sum(gates.astype(jnp.float32)[:, :, None] * onehot.astype(jnp.float32), axis=1)
    weight = jnp.where(jnp.transpose(pick, (2, 0, 1)), table[:, :, None], 0.0)
    weight = weight.astype(jnp.bfloat16)
    chunk = cap // CHUNKS
    mixed = jnp.zeros((tok_rows, width), jnp.float32)
    def ffn(rows):
        rows = rows.reshape(n_experts * chunk, width)
        gate_val = jnp.dot(rows, w_gate[0], preferred_element_type=jnp.float32)
        up_val = jnp.dot(rows, w_up[0], preferred_element_type=jnp.float32)
        hidden = (jax.nn.silu(gate_val) * up_val).astype(jnp.bfloat16)
        result = jnp.dot(hidden, w_down[0], preferred_element_type=jnp.float32)
        return split2(result.reshape(n_experts, chunk, width))

    def combine(part, c, back):
        part_weight = weight[:, :, c * chunk:(c + 1) * chunk].reshape(tok_rows, n_experts * chunk)
        back = back.reshape(n_experts * chunk, width)
        return part + jnp.dot(part_weight, back, preferred_element_type=jnp.float32)

    first = lax.all_to_all(sends[0], "expert", 0, 0, tiled=True)
    group_load = jnp.sum(first[:, 0, width:width + n_experts].astype(jnp.float32), axis=0)
    expert_load = tree_sum(group_load.astype(jnp.int32), "dp")
    second = lax.all_to_all(sends[1], "expert", 0, 0, tiled=True)
    hi0, lo0 = ffn(first[:, :, :width])
    back_hi0 = lax.all_to_all(hi0, "expert", 0, 0, tiled=True)
    hi1, lo1 = ffn(second)
    both = lax.all_to_all(jnp.concatenate([lo0, hi1], axis=1), "expert", 0, 0, tiled=True)
    mixed = combine(mixed, 0, back_hi0)
    mixed = combine(mixed, 0, both[:, :chunk])
    mixed = combine(mixed, 1, both[:, chunk:])
    mixed = lax.optimization_barrier(mixed)
    mixed = combine(mixed, 1, lax.all_to_all(lo1, "expert", 0, 0, tiled=True))
    mixed = mixed.astype(jnp.bfloat16)
    return (mixed, expert_load)


def solution(mesh):
    placed = (
        P(("dp", "expert"), None),
        P(("dp", "expert"), None),
        P(("dp", "expert"), None),
        P("expert", None, None),
        P("expert", None, None),
        P("expert", None, None),
    )
    return jax.shard_map(
        shards,
        mesh=mesh,
        in_specs=placed,
        out_specs=(P(("dp", "expert"), None), P()),
        check_vma=False,
    )
```

```python
import jax
import jax.numpy as jnp
from jax import lax
from jax.experimental import pallas as pl
from jax.sharding import PartitionSpec as P

SRC_CAP = 64
CHUNKS = 2


def split2(value):
    hi = value.astype(jnp.bfloat16)
    lo = (value - hi.astype(jnp.float32)).astype(jnp.bfloat16)
    return hi, lo


def tree_sum(value, axis):
    n_dev = lax.axis_size(axis)
    step = 1
    while step < n_dev:
        perm = [(i, i ^ step) for i in range(n_dev)]
        value = value + lax.ppermute(value, axis, perm)
        step *= 2
    return value


def pack_kernel(pick_ref, tok_ref, load_ref, out_ref):
    n_experts = pick_ref.shape[0]
    tok = tok_ref[...]
    load = load_ref[...]
    for e in range(n_experts):
        packed = jnp.dot(pick_ref[e], tok, preferred_element_type=jnp.float32)
        out_ref[e] = (packed + load).astype(out_ref.dtype)


def pack(pick, tokens, load_row):
    n_experts, chunk, _ = pick.shape
    wide = load_row.shape[1]
    return pl.pallas_call(
        pack_kernel,
        out_shape=jax.ShapeDtypeStruct((n_experts, chunk, wide), tokens.dtype),
    )(pick, tokens, load_row)


def shards(tokens, expert_ids, gates, w_gate, w_up, w_down):
    tok_rows, width = tokens.shape
    n_experts = lax.axis_size("expert")
    cap = SRC_CAP
    experts = jnp.arange(n_experts, dtype=jnp.int32)
    onehot = expert_ids[:, :, None] == experts[None, None, :]
    routed = jnp.any(onehot, axis=1)
    position = jnp.cumsum(routed.astype(jnp.int32), axis=0) - 1
    slots = jnp.arange(cap, dtype=jnp.int32)
    pick = routed.T[:, None, :] & (position.T[:, None, :] == slots[None, :, None])
    local_load = jnp.sum(onehot.astype(jnp.int32), axis=(0, 1))
    wide = -(-(width + n_experts) // 128) * 128
    load_row = jnp.zeros((1, wide), jnp.float32).at[0, width:width + n_experts].set(local_load.astype(jnp.float32))
    half = cap // 2
    pick_bf = pick.astype(jnp.bfloat16)
    sends = (
        pack(pick_bf[:, :half], jnp.pad(tokens, ((0, 0), (0, wide - width))), load_row),
        pack(pick_bf[:, half:], tokens, jnp.zeros((1, width), jnp.float32)),
    )
    table = jnp.sum(gates.astype(jnp.float32)[:, :, None] * onehot.astype(jnp.float32), axis=1)
    weight = jnp.where(jnp.transpose(pick, (2, 0, 1)), table[:, :, None], 0.0)
    weight = weight.astype(jnp.bfloat16)
    chunk = cap // CHUNKS
    mixed = jnp.zeros((tok_rows, width), jnp.float32)
    def ffn(rows):
        rows = rows.reshape(n_experts * chunk, width)
        gate_val = jnp.dot(rows, w_gate[0], preferred_element_type=jnp.float32)
        up_val = jnp.dot(rows, w_up[0], preferred_element_type=jnp.float32)
        hidden = (jax.nn.silu(gate_val) * up_val).astype(jnp.bfloat16)
        result = jnp.dot(hidden, w_down[0], preferred_element_type=jnp.float32)
        return split2(result.reshape(n_experts, chunk, width))

    def combine(part, c, back):
        part_weight = weight[:, :, c * chunk:(c + 1) * chunk].reshape(tok_rows, n_experts * chunk)
        back = back.reshape(n_experts * chunk, width)
        return part + jnp.dot(part_weight, back, preferred_element_type=jnp.float32)

    first = lax.all_to_all(sends[0], "expert", 0, 0, tiled=True)
    group_load = jnp.sum(first[:, 0, width:width + n_experts].astype(jnp.float32), axis=0)
    expert_load = tree_sum(group_load.astype(jnp.int32), "dp")
    second = lax.all_to_all(sends[1], "expert", 0, 0, tiled=True)
    hi0, lo0 = ffn(first[:, :, :width])
    back_hi0 = lax.all_to_all(hi0, "expert", 0, 0, tiled=True)
    hi1, lo1 = ffn(second)
    both = lax.all_to_all(jnp.concatenate([lo0, hi1], axis=1), "expert", 0, 0, tiled=True)
    mixed = combine(mixed, 0, back_hi0)
    mixed = combine(mixed, 0, both[:, :chunk])
    mixed = combine(mixed, 1, both[:, chunk:])
    mixed = combine(mixed, 1, lax.all_to_all(lo1, "expert", 0, 0, tiled=True))
    mixed = mixed.astype(jnp.bfloat16)
    return (mixed, expert_load)


def solution(mesh):
    placed = (
        P(("dp", "expert"), None),
        P(("dp", "expert"), None),
        P(("dp", "expert"), None),
        P("expert", None, None),
        P("expert", None, None),
        P("expert", None, None),
    )
    return jax.shard_map(
        shards,
        mesh=mesh,
        in_specs=placed,
        out_specs=(P(("dp", "expert"), None), P()),
        check_vma=False,
    )
```

```python
import jax
import jax.numpy as jnp
from jax import lax
from jax.experimental import pallas as pl
from jax.sharding import PartitionSpec as P

SRC_CAP = 64
CHUNKS = 2


def split2(value):
    hi = value.astype(jnp.bfloat16)
    lo = (value - hi.astype(jnp.float32)).astype(jnp.bfloat16)
    return hi, lo


def tree_sum(value, axis):
    n_dev = lax.axis_size(axis)
    step = 1
    while step < n_dev:
        perm = [(i, i ^ step) for i in range(n_dev)]
        value = value + lax.ppermute(value, axis, perm)
        step *= 2
    return value


def pack_kernel(pick_ref, tok_ref, load_ref, first_ref, second_ref):
    n_experts, cap, _ = pick_ref.shape
    chunk = cap // 2
    width = second_ref.shape[2]
    tok = tok_ref[...]
    load = load_ref[...]
    for e in range(n_experts):
        packed = jnp.dot(pick_ref[e], tok, preferred_element_type=jnp.float32)
        first_ref[e] = (packed[:chunk] + load).astype(first_ref.dtype)
        second_ref[e] = packed[chunk:, :width].astype(second_ref.dtype)


def pack(pick, tokens, load_row):
    n_experts, cap, _ = pick.shape
    width = tokens.shape[1]
    wide = load_row.shape[1]
    chunk = cap // 2
    return pl.pallas_call(
        pack_kernel,
        out_shape=(
            jax.ShapeDtypeStruct((n_experts, chunk, wide), tokens.dtype),
            jax.ShapeDtypeStruct((n_experts, chunk, width), tokens.dtype),
        ),
    )(pick, jnp.pad(tokens, ((0, 0), (0, wide - width))), load_row)


def shards(tokens, expert_ids, gates, w_gate, w_up, w_down):
    tok_rows, width = tokens.shape
    n_experts = lax.axis_size("expert")
    cap = SRC_CAP
    experts = jnp.arange(n_experts, dtype=jnp.int32)
    onehot = expert_ids[:, :, None] == experts[None, None, :]
    routed = jnp.any(onehot, axis=1)
    position = jnp.cumsum(routed.astype(jnp.int32), axis=0) - 1
    slots = jnp.arange(cap, dtype=jnp.int32)
    pick = routed.T[:, None, :] & (position.T[:, None, :] == slots[None, :, None])
    local_load = jnp.sum(onehot.astype(jnp.int32), axis=(0, 1))
    wide = -(-(width + n_experts) // 128) * 128
    load_row = jnp.zeros((1, wide), jnp.float32).at[0, width:width + n_experts].set(local_load.astype(jnp.float32))
    sends = pack(pick.astype(jnp.bfloat16), tokens, load_row)
    table = jnp.sum(gates.astype(jnp.float32)[:, :, None] * onehot.astype(jnp.float32), axis=1)
    weight = jnp.where(jnp.transpose(pick, (2, 0, 1)), table[:, :, None], 0.0)
    weight = weight.astype(jnp.bfloat16)
    chunk = cap // CHUNKS
    mixed = jnp.zeros((tok_rows, width), jnp.float32)
    def ffn(rows):
        rows = rows.reshape(n_experts * chunk, width)
        gate_val = jnp.dot(rows, w_gate[0], preferred_element_type=jnp.float32)
        up_val = jnp.dot(rows, w_up[0], preferred_element_type=jnp.float32)
        hidden = (jax.nn.silu(gate_val) * up_val).astype(jnp.bfloat16)
        result = jnp.dot(hidden, w_down[0], preferred_element_type=jnp.float32)
        return split2(result.reshape(n_experts, chunk, width))

    def combine(part, c, back):
        part_weight = weight[:, :, c * chunk:(c + 1) * chunk].reshape(tok_rows, n_experts * chunk)
        back = back.reshape(n_experts * chunk, width)
        return part + jnp.dot(part_weight, back, preferred_element_type=jnp.float32)

    first = lax.all_to_all(sends[0], "expert", 0, 0, tiled=True)
    group_load = jnp.sum(first[:, 0, width:width + n_experts].astype(jnp.float32), axis=0)
    expert_load = tree_sum(group_load.astype(jnp.int32), "dp")
    second = lax.all_to_all(sends[1], "expert", 0, 0, tiled=True)
    hi0, lo0 = ffn(first[:, :, :width])
    back_hi0 = lax.all_to_all(hi0, "expert", 0, 0, tiled=True)
    hi1, lo1 = ffn(second)
    both = lax.all_to_all(jnp.concatenate([lo0, hi1], axis=1), "expert", 0, 0, tiled=True)
    mixed = combine(mixed, 0, back_hi0)
    full_weight = weight.reshape(tok_rows, n_experts * cap)
    mixed = mixed + jnp.dot(full_weight, both.reshape(n_experts * cap, width), preferred_element_type=jnp.float32)
    mixed = combine(mixed, 1, lax.all_to_all(lo1, "expert", 0, 0, tiled=True))
    mixed = mixed.astype(jnp.bfloat16)
    return (mixed, expert_load)


def solution(mesh):
    placed = (
        P(("dp", "expert"), None),
        P(("dp", "expert"), None),
        P(("dp", "expert"), None),
        P("expert", None, None),
        P("expert", None, None),
        P("expert", None, None),
    )
    return jax.shard_map(
        shards,
        mesh=mesh,
        in_specs=placed,
        out_specs=(P(("dp", "expert"), None), P()),
        check_vma=False,
    )
```
